512 devices in a mesh: req: 32 (over y, x, core), mlp: 16 (over z).
Axes of the slice: x: 4, y: 4, z: 16, core: 2. Of those that a mesh axis runs over, the one named last changes fastest.
Arguments:
- queries: bfloat16 [12288, 4096], P('req', 'mlp')
- new_keys: bfloat16 [12288, 1024], P(('req', 'mlp')), may hold values from -5 to 5
- new_values: bfloat16 [12288, 1024], P(('req', 'mlp')), may hold values from -6 to 6
- cache_keys: bfloat16 [32, 4096, 1024], P('req', 'mlp')
- cache_values: bfloat16 [32, 4096, 1024], P('req', 'mlp'), may hold values from -6 to 6
- cache_len: int32 [32], P('req'), may hold values from 256 to 4096, as said below
- residual: bfloat16 [12288, 2560], P('req')
- out_weight: bfloat16 [4096, 2560], P('mlp'), may hold values from -0.1796875 to 0.1796875
- norm_gain: bfloat16 [2560], replicated, may hold values from 0.099609375 to 1.8984375
- gate_weight: bfloat16 [2560, 9728], P('req', 'mlp'), may hold values from -0.125 to 0.125
- up_weight: bfloat16 [2560, 9728], P('req', 'mlp'), may hold values from -0.125 to 0.125
- down_weight: bfloat16 [2560, 9728], P('req', 'mlp'), may hold values from -0.0625 to 0.0625
Outputs:
- layer_out: bfloat16 [12288, 2560], P(('req', 'mlp'))
The draws below stay inside these ranges and needn't reach their ends.
Inputs may be any that keep to these rules, and one draw needn't show every extreme that they name: cache_len[r] counts request r's valid cached positions from the first; some request has exactly 4096.
All inputs are finite; a program needn't handle non-finite values.
Results may differ from the reference program's by a relative error of at most 0.012.
Values may be sent and summed in bfloat16 or wider, within the bound.
No kernel may reach another device: no remote copies, remote signals or barrier semaphores. Data moves between devices by JAX's collectives and lax.ppermute only.
A program may use at most 64 MiB of HBM per device.

```python
import math
import jax
import jax.numpy as jnp
from jax import lax

D = 2560
H = 32
KVH = 8
HD = 128
FF = 9728
CACHE_MAX = 4096
SPAN = 384
REQUESTS = 32
TOKENS = 12288
N_MLP = 16


def draw_queries(key, part):
    full_shape = (TOKENS, H * HD)
    values = jnp.clip(jax.random.normal(jax.random.fold_in(key, 11), full_shape, jnp.float32) * 1.6, -5.0, 5.0)
    return values.astype(jnp.bfloat16)


def draw_cache_keys(key, part):
    full_shape = (REQUESTS, CACHE_MAX, KVH * HD)
    values = jnp.clip(jax.random.normal(jax.random.fold_in(key, 13), full_shape, jnp.float32) * 1.6, -5.0, 5.0)
    return values.astype(jnp.bfloat16)


def draw_cache_len(key, part):
    sub_key = jax.random.fold_in(key, 31)
    halving = jax.random.randint(jax.random.fold_in(sub_key, 1), (REQUESTS,), 0, 4)
    lower_bound = jnp.right_shift(jnp.int32(CACHE_MAX), halving + 1)
    upper_bound = jnp.right_shift(jnp.int32(CACHE_MAX), halving) + 1
    lengths = jax.random.randint(jax.random.fold_in(sub_key, 2), (REQUESTS,), lower_bound, upper_bound)
    longest = jax.random.randint(jax.random.fold_in(sub_key, 3), (), 0, REQUESTS)
    return jnp.where(jnp.arange(REQUESTS) == longest, CACHE_MAX, lengths).astype(jnp.int32)


def draw_residual(key, part):
    full_shape = (TOKENS, D)
    sub_key = jax.random.fold_in(key, 53)
    row_scale = jnp.exp(jax.random.uniform(jax.random.fold_in(sub_key, 1), (TOKENS, 1), jnp.float32, math.log(0.3), math.log(3.0)))
    col_scale = jnp.exp(jax.random.uniform(jax.random.fold_in(sub_key, 2), (1, D), jnp.float32, math.log(0.3), math.log(3.0)))
    noise_part = jnp.clip(jax.random.normal(jax.random.fold_in(sub_key, 3), full_shape, jnp.float32), -4.0, 4.0)
    values = noise_part * row_scale * col_scale
    return values.astype(jnp.bfloat16)


def block_levels(own_key, extent, pieces, least, top_value):
    def one(axis_at, shards_of):
        draws = jax.random.uniform(jax.random.fold_in(jax.random.fold_in(own_key, 6), axis_at), (shards_of,), jnp.float32, least / len(pieces), top_value / len(pieces))
        return jnp.repeat(jnp.exp(draws), extent[axis_at] // shards_of).reshape((-1,) + (1,) * (len(extent) - axis_at - 1))

    gain = one(*pieces[0])
    for cut in pieces[1:]:
        gain = gain * one(*cut)
    return gain


def gaussian(own_key, shape, spread, limit, cuts=(), held_as=jnp.bfloat16):
    entries = spread * jax.random.normal(own_key, shape, jnp.float32)
    if cuts:
        entries = entries * block_levels(own_key, shape, cuts, -0.22, 0.18)
    return jnp.clip(entries, -limit, limit).astype(held_as)


def setup_inputs(seed: int = 0) -> dict:
    key_list = jax.random.split(jax.random.key(seed), 13)
    return {
        "queries": draw_queries(jax.random.fold_in(key_list[12], 71), 0),
        "new_keys": gaussian(key_list[1], (TOKENS, KVH * HD), 1.6, 5.0, ((0, 512),)),
        "new_values": gaussian(key_list[2], (TOKENS, KVH * HD), 1.0, 6.0, ((0, 512),)),
        "cache_keys": draw_cache_keys(jax.random.fold_in(key_list[12], 71), 0),
        "cache_values": gaussian(key_list[4], (REQUESTS, CACHE_MAX, KVH * HD), 1.0, 6.0, ((0, 32), (1, 16))),
        "cache_len": draw_cache_len(jax.random.fold_in(key_list[12], 71), 0),
        "residual": draw_residual(jax.random.fold_in(key_list[12], 71), 0),
        "out_weight": gaussian(key_list[7], (H * HD, D), 0.03, 0.1796875, ((0, 16),)),
        "norm_gain": jnp.clip(1.0 + 0.18 * jax.random.normal(key_list[8], (D,), jnp.float32), 0.099609375, 1.8984375).astype(jnp.bfloat16),
        "gate_weight": gaussian(key_list[9], (D, FF), D ** -0.5, 0.125, ((0, 32), (1, 16))),
        "up_weight": gaussian(key_list[10], (D, FF), D ** -0.5, 0.125, ((0, 32), (1, 16))),
        "down_weight": gaussian(key_list[11], (D, FF), FF ** -0.5, 0.0625, ((0, 32), (1, 16))),
    }


norm_eps = 1e-06

def attend(query_rows, keys_cached, values_cached, keys_fresh, values_fresh, length):
    group_size = H // KVH
    key_count = CACHE_MAX + SPAN
    all_keys = jnp.concatenate([keys_cached, keys_fresh], 0).reshape(key_count, KVH, HD).transpose(1, 0, 2)
    all_values = jnp.concatenate([values_cached, values_fresh], 0).reshape(key_count, KVH, HD).transpose(1, 0, 2)
    grouped = query_rows.reshape(SPAN, KVH, group_size, HD).transpose(1, 2, 0, 3)
    key_pos = jnp.arange(key_count).astype(jnp.int32)
    token_pos = jnp.arange(SPAN).astype(jnp.int32)
    allowed = jnp.where(key_pos[None, :] < CACHE_MAX, key_pos[None, :] < length, key_pos[None, :] - CACHE_MAX <= token_pos[:, None])

    def one_head(inputs):
        head_queries, head_keys, head_values = inputs
        scores = jnp.einsum('qtd,kd->qtk', head_queries.astype(jnp.float32), head_keys.astype(jnp.float32)) * HD ** (-0.5)
        scores = jnp.where(allowed[None], scores, -jnp.inf)
        row_max = lax.optimization_barrier(jnp.max(scores, axis=-1, keepdims=True))
        weights = jnp.exp(scores - row_max)
        row_sum = lax.optimization_barrier(jnp.sum(weights, axis=-1, keepdims=True))
        probs = weights.astype(jnp.bfloat16)
        mixed = jnp.einsum('qtk,kd->qtd', probs.astype(jnp.float32), head_values.astype(jnp.float32))
        return (mixed / row_sum).astype(jnp.bfloat16)
    result = lax.map(one_head, (grouped, all_keys, all_values))
    return result.transpose(2, 0, 1, 3).reshape(SPAN, H * HD)

def reference(queries, new_keys, new_values, cache_keys, cache_values, cache_len, residual, out_weight, norm_gain, gate_weight, up_weight, down_weight):
    heads_dev = H // N_MLP
    unit_width = FF // N_MLP
    out_groups = out_weight.reshape(N_MLP, heads_dev * HD, D).astype(jnp.float32)
    down_groups = down_weight.reshape(D, N_MLP, unit_width).astype(jnp.float32)
    gain_full = norm_gain.astype(jnp.float32)

    def one_request(inputs):
        query_rows, keys_cached, values_cached, keys_fresh, values_fresh, length, res_rows = inputs
        attn = attend(query_rows, keys_cached, values_cached, keys_fresh, values_fresh, length)
        head_parts = jnp.einsum('tgk,gkd->gtd', attn.reshape(SPAN, N_MLP, heads_dev * HD).astype(jnp.float32), out_groups)
        attn_proj = lax.optimization_barrier(jnp.sum(lax.optimization_barrier(head_parts.astype(jnp.bfloat16)).astype(jnp.float32), axis=0))
        stream = (res_rows.astype(jnp.float32) + attn_proj).astype(jnp.bfloat16)
        stream_full = stream.astype(jnp.float32)
        factor = lax.rsqrt(lax.optimization_barrier(jnp.mean(stream_full * stream_full, axis=-1, keepdims=True)) + norm_eps)
        normed = (stream_full * factor * gain_full).astype(jnp.bfloat16)
        gate_sum = jnp.dot(normed, gate_weight, preferred_element_type=jnp.float32)
        up_sum = jnp.dot(normed, up_weight, preferred_element_type=jnp.float32)
        hidden = (jax.nn.silu(gate_sum) * up_sum).astype(jnp.bfloat16)
        unit_parts = jnp.einsum('tgf,dgf->gtd', hidden.reshape(SPAN, N_MLP, unit_width).astype(jnp.float32), down_groups)
        mlp_out = lax.optimization_barrier(jnp.sum(lax.optimization_barrier(unit_parts.astype(jnp.bfloat16)).astype(jnp.float32), axis=0))
        return (stream_full + mlp_out).astype(jnp.bfloat16)
    outputs = lax.map(one_request, (queries.reshape(REQUESTS, SPAN, H * HD), cache_keys, cache_values, new_keys.reshape(REQUESTS, SPAN, KVH * HD), new_values.reshape(REQUESTS, SPAN, KVH * HD), cache_len, residual.reshape(REQUESTS, SPAN, D)))
    return outputs.reshape(TOKENS, D)
```

```python
import jax
import jax.numpy as jnp
from jax import lax
from jax.sharding import PartitionSpec as P

H = 32
KVH = 8
HD = 128


norm_eps = 1e-06


def shards(
    queries,
    new_keys,
    new_values,
    cache_keys,
    cache_values,
    cache_len,
    residual,
    out_weight,
    norm_gain,
    gate_weight,
    up_weight,
    down_weight,
):
    n_mlp = lax.axis_size("mlp")
    heads_dev = H // n_mlp
    group_size = H // KVH
    copies = n_mlp // KVH
    assert copies == 2 and heads_dev * copies == group_size
    query_rows = queries.shape[0]
    rows_dev = new_keys.shape[0]
    cache_dev = cache_keys.shape[1]
    cache_half = cache_dev // copies
    new_half = rows_dev // copies
    my_index = lax.axis_index("mlp")
    my_half = my_index % copies

    def to_slots(rows_block, half_rows):
        spread = rows_block.reshape(copies, half_rows, KVH, HD).transpose(1, 2, 0, 3)
        return spread.reshape(half_rows, KVH * copies, HD)

    send = jnp.concatenate(
        [
            to_slots(cache_keys[0], cache_half),
            to_slots(cache_values[0], cache_half),
            to_slots(new_keys, new_half),
            to_slots(new_values, new_half),
        ],
        axis=0,
    )
    arrived = lax.all_to_all(send, "mlp", split_axis=1, concat_axis=0, tiled=True)
    per_src = 2 * cache_half + 2 * new_half
    arrived = arrived.reshape(n_mlp, per_src, HD)
    keys_old = arrived[:, :cache_half].reshape(n_mlp * cache_half, HD)
    values_old = arrived[:, cache_half : 2 * cache_half].reshape(n_mlp * cache_half, HD)
    keys_new = arrived[:, 2 * cache_half : 2 * cache_half + new_half].reshape(n_mlp * new_half, HD)
    values_new = arrived[:, 2 * cache_half + new_half :].reshape(n_mlp * new_half, HD)

    pair = [(d, d ^ 1) for d in range(n_mlp)]
    partner_q = lax.ppermute(queries, "mlp", pair)
    grouped = jnp.concatenate([queries, partner_q], axis=1).reshape(query_rows, group_size, HD)
    score_scale = HD ** (-0.5)

    def absorb(running, key_part, value_part, allowed):
        row_max, row_sum, weighted = running
        scores = (
            jnp.einsum("tqd,kd->qtk", grouped, key_part, preferred_element_type=jnp.float32)
            * score_scale
        )
        scores = jnp.where(allowed, scores, -jnp.inf)
        new_max = jnp.maximum(row_max, jnp.max(scores, axis=-1))
        shrink = jnp.exp(row_max - new_max)
        weights = jnp.exp(scores - new_max[..., None])
        row_sum = row_sum * shrink + jnp.sum(weights, axis=-1)
        weighted = weighted * shrink[..., None] + jnp.einsum(
            "qtk,kd->qtd",
            weights.astype(jnp.bfloat16),
            value_part,
            preferred_element_type=jnp.float32,
        )
        return (new_max, row_sum, weighted)

    start_state = (
        jnp.full((group_size, query_rows), -jnp.inf, jnp.float32),
        jnp.zeros((group_size, query_rows), jnp.float32),
        jnp.zeros((group_size, query_rows, HD), jnp.float32),
    )
    length = cache_len[0]
    cache_count = n_mlp * cache_half
    key_block = min(512, cache_count)

    def cached_positions(idx):
        return (idx // cache_half) * cache_dev + my_half * cache_half + idx % cache_half

    def visit(turn_index, running):
        offset = turn_index * key_block
        key_part = lax.dynamic_slice_in_dim(keys_old, offset, key_block, 0)
        value_part = lax.dynamic_slice_in_dim(values_old, offset, key_block, 0)
        positions = cached_positions(offset + lax.iota(jnp.int32, key_block))
        return absorb(running, key_part, value_part, (positions < length)[None, :])

    running = lax.fori_loop(0, cache_count // key_block, visit, start_state)
    new_idx = lax.iota(jnp.int32, n_mlp * new_half)
    new_pos = (new_idx // new_half) * rows_dev + my_half * new_half + new_idx % new_half
    token_ids = lax.iota(jnp.int32, query_rows)
    causal = new_pos[None, :] <= token_ids[:, None]
    row_max, row_sum, weighted = absorb(running, keys_new, values_new, causal)

    sent = lax.ppermute(
        (weighted[heads_dev:], row_max[heads_dev:], row_sum[heads_dev:]), "mlp", pair
    )
    other_weighted, other_max, other_sum = sent
    mine_max = row_max[:heads_dev]
    top = jnp.maximum(mine_max, other_max)
    scale_a = jnp.exp(mine_max - top)
    scale_b = jnp.exp(other_max - top)
    total = row_sum[:heads_dev] * scale_a + other_sum * scale_b
    mixed = weighted[:heads_dev] * scale_a[..., None] + other_weighted * scale_b[..., None]
    attended = (mixed / total[..., None]).astype(jnp.bfloat16)
    attended = attended.transpose(1, 0, 2).reshape(query_rows, heads_dev * HD)
    partial_value = jnp.dot(attended, out_weight, preferred_element_type=jnp.float32)
    row_start = my_index * rows_dev
    head_sum = lax.psum(partial_value.astype(jnp.bfloat16), "mlp").astype(jnp.float32)
    stream = (residual.astype(jnp.float32) + head_sum).astype(jnp.bfloat16)
    stream_full = stream.astype(jnp.float32)
    factor = lax.rsqrt(jnp.mean(stream_full * stream_full, axis=-1, keepdims=True) + norm_eps)
    normed = (stream_full * factor * norm_gain.astype(jnp.float32)).astype(jnp.bfloat16)
    stream_rows = lax.dynamic_slice_in_dim(stream, row_start, rows_dev, 0)
    gate_sum = jnp.dot(
        normed,
        lax.all_gather(gate_weight, "req", axis=0, tiled=True),
        preferred_element_type=jnp.float32,
    )
    up_sum = jnp.dot(
        normed,
        lax.all_gather(up_weight, "req", axis=0, tiled=True),
        preferred_element_type=jnp.float32,
    )
    hidden = (jax.nn.silu(gate_sum) * up_sum).astype(jnp.bfloat16)
    mlp_part = lax.dot_general(
        hidden,
        lax.all_gather(down_weight, "req", axis=0, tiled=True),
        (((1,), (1,)), ((), ())),
        preferred_element_type=jnp.float32,
    )
    mlp_rows = lax.psum_scatter(
        mlp_part.astype(jnp.bfloat16), "mlp", scatter_dimension=0, tiled=True
    ).astype(jnp.float32)
    return (stream_rows.astype(jnp.float32) + mlp_rows).astype(jnp.bfloat16)


def solution(mesh):
    in_specs = (
        P("req", "mlp"),
        P(("req", "mlp"), None),
        P(("req", "mlp"), None),
        P("req", "mlp", None),
        P("req", "mlp", None),
        P("req"),
        P("req", None),
        P("mlp", None),
        P(),
        P("req", "mlp"),
        P("req", "mlp"),
        P("req", "mlp"),
    )
    out_specs = P(("req", "mlp"), None)
    return jax.shard_map(shards, mesh=mesh, in_specs=in_specs, out_specs=out_specs, check_vma=False)
```

```python
import jax
import jax.numpy as jnp
from jax import lax
from jax.sharding import PartitionSpec as P

H = 32
KVH = 8
HD = 128


norm_eps = 1e-06


def shards(
    queries,
    new_keys,
    new_values,
    cache_keys,
    cache_values,
    cache_len,
    residual,
    out_weight,
    norm_gain,
    gate_weight,
    up_weight,
    down_weight,
):
    n_mlp = lax.axis_size("mlp")
    heads_dev = H // n_mlp
    group_size = H // KVH
    copies = n_mlp // KVH
    assert copies == 2 and heads_dev * copies == group_size
    query_rows = queries.shape[0]
    rows_dev = new_keys.shape[0]
    cache_dev = cache_keys.shape[1]
    cache_half = cache_dev // copies
    new_half = rows_dev // copies
    my_index = lax.axis_index("mlp")
    my_half = my_index % copies

    def to_slots(rows_block, half_rows):
        spread = rows_block.reshape(copies, half_rows, KVH, HD).transpose(1, 2, 0, 3)
        return spread.reshape(half_rows, KVH * copies, HD)

    send = jnp.concatenate(
        [
            to_slots(cache_keys[0], cache_half),
            to_slots(cache_values[0], cache_half),
            to_slots(new_keys, new_half),
            to_slots(new_values, new_half),
        ],
        axis=0,
    )
    arrived = lax.all_to_all(send, "mlp", split_axis=1, concat_axis=0, tiled=True)
    per_src = 2 * cache_half + 2 * new_half
    arrived = arrived.reshape(n_mlp, per_src, HD)
    keys_old = arrived[:, :cache_half].reshape(n_mlp * cache_half, HD)
    values_old = arrived[:, cache_half : 2 * cache_half].reshape(n_mlp * cache_half, HD)
    keys_new = arrived[:, 2 * cache_half : 2 * cache_half + new_half].reshape(n_mlp * new_half, HD)
    values_new = arrived[:, 2 * cache_half + new_half :].reshape(n_mlp * new_half, HD)

    pair = [(d, d ^ 1) for d in range(n_mlp)]
    partner_q = lax.ppermute(queries, "mlp", pair)
    grouped = jnp.concatenate([queries, partner_q], axis=1).reshape(query_rows, group_size, HD)
    score_scale = HD ** (-0.5)

    def absorb(running, key_part, value_part, allowed):
        row_max, row_sum, weighted = running
        scores = (
            jnp.einsum("tqd,kd->qtk", grouped, key_part, preferred_element_type=jnp.float32)
            * score_scale
        )
        scores = jnp.where(allowed, scores, -jnp.inf)
        new_max = jnp.maximum(row_max, jnp.max(scores, axis=-1))
        shrink = jnp.exp(row_max - new_max)
        weights = jnp.exp(scores - new_max[..., None])
        row_sum = row_sum * shrink + jnp.sum(weights, axis=-1)
        weighted = weighted * shrink[..., None] + jnp.einsum(
            "qtk,kd->qtd",
            weights.astype(jnp.bfloat16),
            value_part,
            preferred_element_type=jnp.float32,
        )
        return (new_max, row_sum, weighted)

    start_state = (
        jnp.full((group_size, query_rows), -jnp.inf, jnp.float32),
        jnp.zeros((group_size, query_rows), jnp.float32),
        jnp.zeros((group_size, query_rows, HD), jnp.float32),
    )
    length = cache_len[0]
    cache_count = n_mlp * cache_half
    key_block = min(512, cache_count)

    def cached_positions(idx):
        return (idx // cache_half) * cache_dev + my_half * cache_half + idx % cache_half

    def visit(turn_index, running):
        offset = turn_index * key_block
        key_part = lax.dynamic_slice_in_dim(keys_old, offset, key_block, 0)
        value_part = lax.dynamic_slice_in_dim(values_old, offset, key_block, 0)
        positions = cached_positions(offset + lax.iota(jnp.int32, key_block))
        return absorb(running, key_part, value_part, (positions < length)[None, :])

    running = lax.fori_loop(0, cache_count // key_block, visit, start_state)
    new_idx = lax.iota(jnp.int32, n_mlp * new_half)
    new_pos = (new_idx // new_half) * rows_dev + my_half * new_half + new_idx % new_half
    token_ids = lax.iota(jnp.int32, query_rows)
    causal = new_pos[None, :] <= token_ids[:, None]
    row_max, row_sum, weighted = absorb(running, keys_new, values_new, causal)

    sent = lax.ppermute(
        (weighted[heads_dev:], row_max[heads_dev:], row_sum[heads_dev:]), "mlp", pair
    )
    other_weighted, other_max, other_sum = sent
    mine_max = row_max[:heads_dev]
    top = jnp.maximum(mine_max, other_max)
    scale_a = jnp.exp(mine_max - top)
    scale_b = jnp.exp(other_max - top)
    total = row_sum[:heads_dev] * scale_a + other_sum * scale_b
    mixed = weighted[:heads_dev] * scale_a[..., None] + other_weighted * scale_b[..., None]
    attended = (mixed / total[..., None]).astype(jnp.bfloat16)
    attended = attended.transpose(1, 0, 2).reshape(query_rows, heads_dev * HD)
    partial_value = jnp.dot(attended, out_weight, preferred_element_type=jnp.float32)
    row_start = my_index * rows_dev
    head_sum = lax.psum(partial_value.astype(jnp.bfloat16), "mlp").astype(jnp.float32)
    stream = (residual.astype(jnp.float32) + head_sum).astype(jnp.bfloat16)
    stream_full = stream.astype(jnp.float32)
    factor = lax.rsqrt(jnp.mean(stream_full * stream_full, axis=-1, keepdims=True) + norm_eps)
    normed = (stream_full * factor * norm_gain.astype(jnp.float32)).astype(jnp.bfloat16)
    stream_rows = lax.dynamic_slice_in_dim(stream, row_start, rows_dev, 0)
    units = gate_weight.shape[1]
    weights_full = lax.all_gather(
        jnp.concatenate([gate_weight, up_weight, down_weight], axis=1), "req", axis=0, tiled=True
    )
    gate_sum = jnp.dot(normed, weights_full[:, :units], preferred_element_type=jnp.float32)
    up_sum = jnp.dot(normed, weights_full[:, units : 2 * units], preferred_element_type=jnp.float32)
    hidden = (jax.nn.silu(gate_sum) * up_sum).astype(jnp.bfloat16)
    mlp_part = lax.dot_general(
        hidden,
        weights_full[:, 2 * units :],
        (((1,), (1,)), ((), ())),
        preferred_element_type=jnp.float32,
    )
    mlp_rows = lax.psum_scatter(
        mlp_part.astype(jnp.bfloat16), "mlp", scatter_dimension=0, tiled=True
    ).astype(jnp.float32)
    return (stream_rows.astype(jnp.float32) + mlp_rows).astype(jnp.bfloat16)


def solution(mesh):
    in_specs = (
        P("req", "mlp"),
        P(("req", "mlp"), None),
        P(("req", "mlp"), None),
        P("req", "mlp", None),
        P("req", "mlp", None),
        P("req"),
        P("req", None),
        P("mlp", None),
        P(),
        P("req", "mlp"),
        P("req", "mlp"),
        P("req", "mlp"),
    )
    out_specs = P(("req", "mlp"), None)
    return jax.shard_map(shards, mesh=mesh, in_specs=in_specs, out_specs=out_specs, check_vma=False)
```

```python
import jax
import jax.numpy as jnp
from jax import lax
from jax.sharding import PartitionSpec as P

H = 32
KVH = 8
HD = 128


norm_eps = 1e-06


def shards(
    queries,
    new_keys,
    new_values,
    cache_keys,
    cache_values,
    cache_len,
    residual,
    out_weight,
    norm_gain,
    gate_weight,
    up_weight,
    down_weight,
):
    n_mlp = lax.axis_size("mlp")
    heads_dev = H // n_mlp
    group_size = H // KVH
    copies = n_mlp // KVH
    assert copies == 2 and heads_dev * copies == group_size
    query_rows = queries.shape[0]
    rows_dev = new_keys.shape[0]
    cache_dev = cache_keys.shape[1]
    cache_half = cache_dev // copies
    new_half = rows_dev // copies
    my_index = lax.axis_index("mlp")
    my_half = my_index % copies

    def to_slots(rows_block, half_rows):
        spread = rows_block.reshape(copies, half_rows, KVH, HD).transpose(1, 2, 0, 3)
        return spread.reshape(half_rows, KVH * copies, HD)

    send = jnp.concatenate(
        [
            to_slots(cache_keys[0], cache_half),
            to_slots(cache_values[0], cache_half),
            to_slots(new_keys, new_half),
            to_slots(new_values, new_half),
        ],
        axis=0,
    )
    arrived = lax.all_to_all(send, "mlp", split_axis=1, concat_axis=0, tiled=True)
    per_src = 2 * cache_half + 2 * new_half
    arrived = arrived.reshape(n_mlp, per_src, HD)
    keys_old = arrived[:, :cache_half].reshape(n_mlp * cache_half, HD)
    values_old = arrived[:, cache_half : 2 * cache_half].reshape(n_mlp * cache_half, HD)
    keys_new = arrived[:, 2 * cache_half : 2 * cache_half + new_half].reshape(n_mlp * new_half, HD)
    values_new = arrived[:, 2 * cache_half + new_half :].reshape(n_mlp * new_half, HD)

    pair = [(d, d ^ 1) for d in range(n_mlp)]
    partner_q = lax.ppermute(queries, "mlp", pair)
    score_scale = HD ** (-0.5)
    chunk_spans = [(0, 16), (16, rows_dev - 16)] if rows_dev > 16 else [(0, rows_dev)]
    n_chunks = len(chunk_spans)

    def chunk_of(rows, c):
        first, size = chunk_spans[c]
        split = rows.reshape((n_mlp, rows_dev) + rows.shape[1:])[:, first : first + size]
        return split.reshape((n_mlp * size,) + rows.shape[1:])

    def absorb(grouped, running, key_part, value_part, allowed):
        row_max, row_sum, weighted = running
        scores = (
            jnp.einsum("tqd,kd->qtk", grouped, key_part, preferred_element_type=jnp.float32)
            * score_scale
        )
        scores = jnp.where(allowed, scores, -jnp.inf)
        new_max = jnp.maximum(row_max, jnp.max(scores, axis=-1))
        shrink = jnp.exp(row_max - new_max)
        weights = jnp.exp(scores - new_max[..., None])
        row_sum = row_sum * shrink + jnp.sum(weights, axis=-1)
        weighted = weighted * shrink[..., None] + jnp.einsum(
            "qtk,kd->qtd",
            weights.astype(jnp.bfloat16),
            value_part,
            preferred_element_type=jnp.float32,
        )
        return (new_max, row_sum, weighted)

    length = cache_len[0]
    cache_count = n_mlp * cache_half
    key_block = min(512, cache_count)

    def cached_positions(idx):
        return (idx // cache_half) * cache_dev + my_half * cache_half + idx % cache_half

    new_idx = lax.iota(jnp.int32, n_mlp * new_half)
    new_pos = (new_idx // new_half) * rows_dev + my_half * new_half + new_idx % new_half
    token_all = lax.iota(jnp.int32, query_rows)
    units = gate_weight.shape[1]
    weights_full = lax.all_gather(
        jnp.concatenate([gate_weight, up_weight, down_weight], axis=1), "req", axis=0, tiled=True
    )
    gain = norm_gain.astype(jnp.float32)
    outs = []
    for c in range(n_chunks):
        chunk_q = jnp.concatenate([chunk_of(queries, c), chunk_of(partner_q, c)], axis=1)
        chunk_rows = chunk_q.shape[0]
        grouped = chunk_q.reshape(chunk_rows, group_size, HD)
        start_state = (
            jnp.full((group_size, chunk_rows), -jnp.inf, jnp.float32),
            jnp.zeros((group_size, chunk_rows), jnp.float32),
            jnp.zeros((group_size, chunk_rows, HD), jnp.float32),
        )

        def visit(turn_index, running, grouped=grouped):
            offset = turn_index * key_block
            key_part = lax.dynamic_slice_in_dim(keys_old, offset, key_block, 0)
            value_part = lax.dynamic_slice_in_dim(values_old, offset, key_block, 0)
            positions = cached_positions(offset + lax.iota(jnp.int32, key_block))
            return absorb(grouped, running, key_part, value_part, (positions < length)[None, :])

        running = lax.fori_loop(0, cache_count // key_block, visit, start_state)
        causal = new_pos[None, :] <= chunk_of(token_all, c)[:, None]
        row_max, row_sum, weighted = absorb(grouped, running, keys_new, values_new, causal)

        sent = lax.ppermute(
            (weighted[heads_dev:], row_max[heads_dev:], row_sum[heads_dev:]), "mlp", pair
        )
        other_weighted, other_max, other_sum = sent
        mine_max = row_max[:heads_dev]
        top = jnp.maximum(mine_max, other_max)
        scale_a = jnp.exp(mine_max - top)
        scale_b = jnp.exp(other_max - top)
        total = row_sum[:heads_dev] * scale_a + other_sum * scale_b
        mixed = weighted[:heads_dev] * scale_a[..., None] + other_weighted * scale_b[..., None]
        attended = (mixed / total[..., None]).astype(jnp.bfloat16)
        attended = attended.transpose(1, 0, 2).reshape(chunk_rows, heads_dev * HD)
        partial_value = jnp.dot(attended, out_weight, preferred_element_type=jnp.float32)
        head_rows = lax.psum_scatter(
            partial_value.astype(jnp.bfloat16), "mlp", scatter_dimension=0, tiled=True
        ).astype(jnp.float32)
        first, size = chunk_spans[c]
        res_rows = lax.dynamic_slice_in_dim(residual, my_index * rows_dev + first, size, 0)
        stream = (res_rows.astype(jnp.float32) + head_rows).astype(jnp.bfloat16)
        stream_full = stream.astype(jnp.float32)
        factor = lax.rsqrt(jnp.mean(stream_full * stream_full, axis=-1, keepdims=True) + norm_eps)
        normed = (stream_full * factor * gain).astype(jnp.bfloat16)
        normed_all = lax.all_gather(normed, "mlp", axis=0, tiled=True)
        gate_sum = jnp.dot(normed_all, weights_full[:, :units], preferred_element_type=jnp.float32)
        up_sum = jnp.dot(
            normed_all, weights_full[:, units : 2 * units], preferred_element_type=jnp.float32
        )
        hidden = (jax.nn.silu(gate_sum) * up_sum).astype(jnp.bfloat16)
        mlp_part = lax.dot_general(
            hidden,
            weights_full[:, 2 * units :],
            (((1,), (1,)), ((), ())),
            preferred_element_type=jnp.float32,
        )
        mlp_rows = lax.psum_scatter(
            mlp_part.astype(jnp.bfloat16), "mlp", scatter_dimension=0, tiled=True
        ).astype(jnp.float32)
        outs.append((stream_full + mlp_rows).astype(jnp.bfloat16))
    return jnp.concatenate(outs, axis=0)


def solution(mesh):
    in_specs = (
        P("req", "mlp"),
        P(("req", "mlp"), None),
        P(("req", "mlp"), None),
        P("req", "mlp", None),
        P("req", "mlp", None),
        P("req"),
        P("req", None),
        P("mlp", None),
        P(),
        P("req", "mlp"),
        P("req", "mlp"),
        P("req", "mlp"),
    )
    out_specs = P(("req", "mlp"), None)
    return jax.shard_map(shards, mesh=mesh, in_specs=in_specs, out_specs=out_specs, check_vma=False)
```

```python
import jax
import jax.numpy as jnp
from jax import lax
from jax.sharding import PartitionSpec as P

H = 32
KVH = 8
HD = 128


norm_eps = 1e-06


def shards(
    queries,
    new_keys,
    new_values,
    cache_keys,
    cache_values,
    cache_len,
    residual,
    out_weight,
    norm_gain,
    gate_weight,
    up_weight,
    down_weight,
):
    n_mlp = lax.axis_size("mlp")
    heads_dev = H // n_mlp
    group_size = H // KVH
    copies = n_mlp // KVH
    assert copies == 2 and heads_dev * copies == group_size
    query_rows = queries.shape[0]
    rows_dev = new_keys.shape[0]
    cache_dev = cache_keys.shape[1]
    cache_half = cache_dev // copies
    new_half = rows_dev // copies
    my_index = lax.axis_index("mlp")
    my_half = my_index % copies

    def to_slots(rows_block, half_rows):
        spread = rows_block.reshape(copies, half_rows, KVH, HD).transpose(1, 2, 0, 3)
        return spread.reshape(half_rows, KVH * copies, HD)

    send = jnp.concatenate(
        [
            to_slots(cache_keys[0], cache_half),
            to_slots(cache_values[0], cache_half),
            to_slots(new_keys, new_half),
            to_slots(new_values, new_half),
        ],
        axis=0,
    )
    arrived = lax.all_to_all(send, "mlp", split_axis=1, concat_axis=0, tiled=True)
    per_src = 2 * cache_half + 2 * new_half
    arrived = arrived.reshape(n_mlp, per_src, HD)
    keys_old = arrived[:, :cache_half].reshape(n_mlp * cache_half, HD)
    values_old = arrived[:, cache_half : 2 * cache_half].reshape(n_mlp * cache_half, HD)
    keys_new = arrived[:, 2 * cache_half : 2 * cache_half + new_half].reshape(n_mlp * new_half, HD)
    values_new = arrived[:, 2 * cache_half + new_half :].reshape(n_mlp * new_half, HD)

    pair = [(d, d ^ 1) for d in range(n_mlp)]
    partner_q = lax.ppermute(queries, "mlp", pair)
    grouped = jnp.concatenate([queries, partner_q], axis=1).reshape(query_rows, group_size, HD)
    score_scale = HD ** (-0.5)

    length = cache_len[0]
    cache_count = n_mlp * cache_half
    keys_all = jnp.concatenate([keys_old, keys_new], axis=0)
    values_all = jnp.concatenate([values_old, values_new], axis=0)
    cached_idx = lax.iota(jnp.int32, cache_count)
    cached_pos = (cached_idx // cache_half) * cache_dev + my_half * cache_half + cached_idx % cache_half
    new_idx = lax.iota(jnp.int32, n_mlp * new_half)
    new_pos = (new_idx // new_half) * rows_dev + my_half * new_half + new_idx % new_half
    token_ids = lax.iota(jnp.int32, query_rows)
    allowed = jnp.concatenate(
        [
            jnp.broadcast_to((cached_pos < length)[None, :], (query_rows, cache_count)),
            new_pos[None, :] <= token_ids[:, None],
        ],
        axis=1,
    )
    scores = (
        jnp.einsum("tqd,kd->qtk", grouped, keys_all, preferred_element_type=jnp.float32)
        * score_scale
    )
    scores = jnp.where(allowed[None], scores, -jnp.inf)
    row_max = jnp.max(scores, axis=-1)
    weights = jnp.exp(scores - row_max[..., None])
    row_sum = jnp.sum(weights, axis=-1)
    weighted = jnp.einsum(
        "qtk,kd->qtd", weights.astype(jnp.bfloat16), values_all, preferred_element_type=jnp.float32
    )

    sent = lax.ppermute(
        (weighted[heads_dev:], row_max[heads_dev:], row_sum[heads_dev:]), "mlp", pair
    )
    other_weighted, other_max, other_sum = sent
    mine_max = row_max[:heads_dev]
    top = jnp.maximum(mine_max, other_max)
    scale_a = jnp.exp(mine_max - top)
    scale_b = jnp.exp(other_max - top)
    total = row_sum[:heads_dev] * scale_a + other_sum * scale_b
    mixed = weighted[:heads_dev] * scale_a[..., None] + other_weighted * scale_b[..., None]
    attended = (mixed / total[..., None]).astype(jnp.bfloat16)
    attended = attended.transpose(1, 0, 2).reshape(query_rows, heads_dev * HD)
    partial_value = jnp.dot(attended, out_weight, preferred_element_type=jnp.float32)
    row_start = my_index * rows_dev
    head_sum = lax.psum(partial_value.astype(jnp.bfloat16), "mlp").astype(jnp.float32)
    stream = (residual.astype(jnp.float32) + head_sum).astype(jnp.bfloat16)
    stream_full = stream.astype(jnp.float32)
    factor = lax.rsqrt(jnp.mean(stream_full * stream_full, axis=-1, keepdims=True) + norm_eps)
    normed = (stream_full * factor * norm_gain.astype(jnp.float32)).astype(jnp.bfloat16)
    stream_rows = lax.dynamic_slice_in_dim(stream, row_start, rows_dev, 0)
    units = gate_weight.shape[1]
    weights_full = lax.all_gather(
        jnp.concatenate([gate_weight, up_weight, down_weight], axis=1), "req", axis=0, tiled=True
    )
    gate_sum = jnp.dot(normed, weights_full[:, :units], preferred_element_type=jnp.float32)
    up_sum = jnp.dot(normed, weights_full[:, units : 2 * units], preferred_element_type=jnp.float32)
    hidden = (jax.nn.silu(gate_sum) * up_sum).astype(jnp.bfloat16)
    mlp_part = lax.dot_general(
        hidden,
        weights_full[:, 2 * units :],
        (((1,), (1,)), ((), ())),
        preferred_element_type=jnp.float32,
    )
    mlp_rows = lax.psum_scatter(
        mlp_part.astype(jnp.bfloat16), "mlp", scatter_dimension=0, tiled=True
    ).astype(jnp.float32)
    return (stream_rows.astype(jnp.float32) + mlp_rows).astype(jnp.bfloat16)


def solution(mesh):
    in_specs = (
        P("req", "mlp"),
        P(("req", "mlp"), None),
        P(("req", "mlp"), None),
        P("req", "mlp", None),
        P("req", "mlp", None),
        P("req"),
        P("req", None),
        P("mlp", None),
        P(),
        P("req", "mlp"),
        P("req", "mlp"),
        P("req", "mlp"),
    )
    out_specs = P(("req", "mlp"), None)
    return jax.shard_map(shards, mesh=mesh, in_specs=in_specs, out_specs=out_specs, check_vma=False)
```

```python
import jax
import jax.numpy as jnp
from jax import lax
from jax.sharding import PartitionSpec as P

H = 32
KVH = 8
HD = 128


norm_eps = 1e-06


def shards(
    queries,
    new_keys,
    new_values,
    cache_keys,
    cache_values,
    cache_len,
    residual,
    out_weight,
    norm_gain,
    gate_weight,
    up_weight,
    down_weight,
):
    n_mlp = lax.axis_size("mlp")
    heads_dev = H // n_mlp
    group_size = H // KVH
    copies = n_mlp // KVH
    assert copies == 2 and heads_dev * copies == group_size
    query_rows = queries.shape[0]
    rows_dev = new_keys.shape[0]
    cache_dev = cache_keys.shape[1]
    cache_half = cache_dev // copies
    new_half = rows_dev // copies
    my_index = lax.axis_index("mlp")
    my_half = my_index % copies

    def to_slots(rows_block, half_rows):
        spread = rows_block.reshape(copies, half_rows, KVH, HD).transpose(1, 2, 0, 3)
        return spread.reshape(half_rows, KVH * copies, HD)

    send = jnp.concatenate(
        [
            to_slots(cache_keys[0], cache_half),
            to_slots(cache_values[0], cache_half),
            to_slots(new_keys, new_half),
            to_slots(new_values, new_half),
        ],
        axis=0,
    )
    arrived = lax.all_to_all(send, "mlp", split_axis=1, concat_axis=0, tiled=True)
    per_src = 2 * cache_half + 2 * new_half
    arrived = arrived.reshape(n_mlp, per_src, HD)
    keys_old = arrived[:, :cache_half].reshape(n_mlp * cache_half, HD)
    values_old = arrived[:, cache_half : 2 * cache_half].reshape(n_mlp * cache_half, HD)
    keys_new = arrived[:, 2 * cache_half : 2 * cache_half + new_half].reshape(n_mlp * new_half, HD)
    values_new = arrived[:, 2 * cache_half + new_half :].reshape(n_mlp * new_half, HD)

    pair = [(d, d ^ 1) for d in range(n_mlp)]
    partner_q = lax.ppermute(queries, "mlp", pair)
    grouped = jnp.concatenate([queries, partner_q], axis=1).reshape(query_rows, group_size, HD)
    score_scale = HD ** (-0.5)

    length = cache_len[0]
    cache_count = n_mlp * cache_half
    keys_all = jnp.concatenate([keys_old, keys_new], axis=0)
    values_all = jnp.concatenate([values_old, values_new], axis=0)
    cached_idx = lax.iota(jnp.int32, cache_count)
    cached_pos = (cached_idx // cache_half) * cache_dev + my_half * cache_half + cached_idx % cache_half
    new_idx = lax.iota(jnp.int32, n_mlp * new_half)
    new_pos = (new_idx // new_half) * rows_dev + my_half * new_half + new_idx % new_half
    token_ids = lax.iota(jnp.int32, query_rows)
    allowed = jnp.concatenate(
        [
            jnp.broadcast_to((cached_pos < length)[None, :], (query_rows, cache_count)),
            new_pos[None, :] <= token_ids[:, None],
        ],
        axis=1,
    )
    scores = (
        jnp.einsum("tqd,kd->qtk", grouped, keys_all, preferred_element_type=jnp.float32)
        * score_scale
    )
    scores = jnp.where(allowed[None], scores, -jnp.inf)
    row_max = jnp.max(scores, axis=-1)
    weights = jnp.exp(scores - row_max[..., None])
    row_sum = jnp.sum(weights, axis=-1)
    weighted = jnp.einsum(
        "qtk,kd->qtd", weights.astype(jnp.bfloat16), values_all, preferred_element_type=jnp.float32
    )

    stats_rows = 2 * query_rows // HD
    packed = jnp.concatenate(
        [
            weighted[heads_dev:],
            jnp.stack([row_max[heads_dev:], row_sum[heads_dev:]], axis=1).reshape(
                heads_dev, stats_rows, HD
            ),
        ],
        axis=1,
    )
    sent = lax.ppermute(packed, "mlp", pair)
    other_weighted = sent[:, :query_rows]
    other_stats = sent[:, query_rows:].reshape(heads_dev, 2, query_rows)
    other_max = other_stats[:, 0]
    other_sum = other_stats[:, 1]
    mine_max = row_max[:heads_dev]
    top = jnp.maximum(mine_max, other_max)
    scale_a = jnp.exp(mine_max - top)
    scale_b = jnp.exp(other_max - top)
    total = row_sum[:heads_dev] * scale_a + other_sum * scale_b
    mixed = weighted[:heads_dev] * scale_a[..., None] + other_weighted * scale_b[..., None]
    attended = (mixed / total[..., None]).astype(jnp.bfloat16)
    attended = attended.transpose(1, 0, 2).reshape(query_rows, heads_dev * HD)
    partial_value = jnp.dot(attended, out_weight, preferred_element_type=jnp.float32)
    row_start = my_index * rows_dev
    head_sum = lax.psum(partial_value.astype(jnp.bfloat16), "mlp").astype(jnp.float32)
    stream = (residual.astype(jnp.float32) + head_sum).astype(jnp.bfloat16)
    stream_full = stream.astype(jnp.float32)
    factor = lax.rsqrt(jnp.mean(stream_full * stream_full, axis=-1, keepdims=True) + norm_eps)
    normed = (stream_full * factor * norm_gain.astype(jnp.float32)).astype(jnp.bfloat16)
    stream_rows = lax.dynamic_slice_in_dim(stream, row_start, rows_dev, 0)
    units = gate_weight.shape[1]
    weights_full = lax.all_gather(
        jnp.concatenate([gate_weight, up_weight, down_weight], axis=1), "req", axis=0, tiled=True
    )
    gate_sum = jnp.dot(normed, weights_full[:, :units], preferred_element_type=jnp.float32)
    up_sum = jnp.dot(normed, weights_full[:, units : 2 * units], preferred_element_type=jnp.float32)
    hidden = (jax.nn.silu(gate_sum) * up_sum).astype(jnp.bfloat16)
    mlp_part = lax.dot_general(
        hidden,
        weights_full[:, 2 * units :],
        (((1,), (1,)), ((), ())),
        preferred_element_type=jnp.float32,
    )
    mlp_rows = lax.psum_scatter(
        mlp_part.astype(jnp.bfloat16), "mlp", scatter_dimension=0, tiled=True
    ).astype(jnp.float32)
    return (stream_rows.astype(jnp.float32) + mlp_rows).astype(jnp.bfloat16)


def solution(mesh):
    in_specs = (
        P("req", "mlp"),
        P(("req", "mlp"), None),
        P(("req", "mlp"), None),
        P("req", "mlp", None),
        P("req", "mlp", None),
        P("req"),
        P("req", None),
        P("mlp", None),
        P(),
        P("req", "mlp"),
        P("req", "mlp"),
        P("req", "mlp"),
    )
    out_specs = P(("req", "mlp"), None)
    return jax.shard_map(shards, mesh=mesh, in_specs=in_specs, out_specs=out_specs, check_vma=False)
```

```python
import jax
import jax.numpy as jnp
from jax import lax
from jax.sharding import PartitionSpec as P

H = 32
KVH = 8
HD = 128


norm_eps = 1e-06


def shards(
    queries,
    new_keys,
    new_values,
    cache_keys,
    cache_values,
    cache_len,
    residual,
    out_weight,
    norm_gain,
    gate_weight,
    up_weight,
    down_weight,
):
    n_mlp = lax.axis_size("mlp")
    heads_dev = H // n_mlp
    group_size = H // KVH
    copies = n_mlp // KVH
    assert copies == 2 and heads_dev * copies == group_size
    query_rows = queries.shape[0]
    rows_dev = new_keys.shape[0]
    cache_dev = cache_keys.shape[1]
    cache_half = cache_dev // copies
    new_half = rows_dev // copies
    my_index = lax.axis_index("mlp")
    my_half = my_index % copies

    def to_slots(rows_block, half_rows):
        spread = rows_block.reshape(copies, half_rows, KVH, HD).transpose(1, 2, 0, 3)
        return spread.reshape(half_rows, KVH * copies, HD)

    send = jnp.concatenate(
        [
            to_slots(cache_keys[0], cache_half),
            to_slots(cache_values[0], cache_half),
            to_slots(new_keys, new_half),
            to_slots(new_values, new_half),
        ],
        axis=0,
    )
    arrived = lax.all_to_all(send, "mlp", split_axis=1, concat_axis=0, tiled=True)
    per_src = 2 * cache_half + 2 * new_half
    arrived = arrived.reshape(n_mlp, per_src, HD)
    keys_old = arrived[:, :cache_half].reshape(n_mlp * cache_half, HD)
    values_old = arrived[:, cache_half : 2 * cache_half].reshape(n_mlp * cache_half, HD)
    keys_new = arrived[:, 2 * cache_half : 2 * cache_half + new_half].reshape(n_mlp * new_half, HD)
    values_new = arrived[:, 2 * cache_half + new_half :].reshape(n_mlp * new_half, HD)

    pair = [(d, d ^ 1) for d in range(n_mlp)]
    partner_q = lax.ppermute(queries, "mlp", pair)
    grouped = jnp.concatenate([queries, partner_q], axis=1).reshape(query_rows, group_size, HD)
    score_scale = HD ** (-0.5)

    length = cache_len[0]
    cache_count = n_mlp * cache_half
    keys_all = jnp.concatenate([keys_old, keys_new], axis=0)
    values_all = jnp.concatenate([values_old, values_new], axis=0)
    cached_idx = lax.iota(jnp.int32, cache_count)
    cached_pos = (cached_idx // cache_half) * cache_dev + my_half * cache_half + cached_idx % cache_half
    new_idx = lax.iota(jnp.int32, n_mlp * new_half)
    new_pos = (new_idx // new_half) * rows_dev + my_half * new_half + new_idx % new_half
    token_ids = lax.iota(jnp.int32, query_rows)
    allowed = jnp.concatenate(
        [
            jnp.broadcast_to((cached_pos < length)[None, :], (query_rows, cache_count)),
            new_pos[None, :] <= token_ids[:, None],
        ],
        axis=1,
    )
    scores = (
        jnp.einsum("tqd,kd->qtk", grouped, keys_all, preferred_element_type=jnp.float32)
        * score_scale
    )
    scores = jnp.where(allowed[None], scores, -jnp.inf)
    row_max = jnp.max(scores, axis=-1)
    weights = jnp.exp(scores - row_max[..., None])
    row_sum = jnp.sum(weights, axis=-1)
    weighted = jnp.einsum(
        "qtk,kd->qtd", weights.astype(jnp.bfloat16), values_all, preferred_element_type=jnp.float32
    )

    sent = lax.ppermute(
        (weighted[heads_dev:], row_max[heads_dev:], row_sum[heads_dev:]), "mlp", pair
    )
    other_weighted, other_max, other_sum = sent
    mine_max = row_max[:heads_dev]
    top = jnp.maximum(mine_max, other_max)
    scale_a = jnp.exp(mine_max - top)
    scale_b = jnp.exp(other_max - top)
    total = row_sum[:heads_dev] * scale_a + other_sum * scale_b
    mixed = weighted[:heads_dev] * scale_a[..., None] + other_weighted * scale_b[..., None]
    attended = (mixed / total[..., None]).astype(jnp.bfloat16)
    attended = attended.transpose(1, 0, 2).reshape(query_rows, heads_dev * HD)
    partial_value = jnp.dot(attended, out_weight, preferred_element_type=jnp.float32)
    row_start = my_index * rows_dev
    head_sum = lax.psum(partial_value.astype(jnp.bfloat16), "mlp").astype(jnp.float32)
    stream = (residual.astype(jnp.float32) + head_sum).astype(jnp.bfloat16)
    stream_full = stream.astype(jnp.float32)
    factor = lax.rsqrt(jnp.mean(stream_full * stream_full, axis=-1, keepdims=True) + norm_eps)
    normed = (stream_full * factor * norm_gain.astype(jnp.float32)).astype(jnp.bfloat16)
    stream_rows = lax.dynamic_slice_in_dim(stream, row_start, rows_dev, 0)
    units = gate_weight.shape[1]
    width = -(-units // 128) * 128

    def padded(block):
        return jnp.pad(block, ((0, 0), (0, width - units)))

    weights_full = lax.all_gather(
        jnp.concatenate([padded(gate_weight), padded(up_weight), padded(down_weight)], axis=1),
        "req",
        axis=0,
        tiled=True,
    )
    gate_sum = jnp.dot(normed, weights_full[:, :units], preferred_element_type=jnp.float32)
    up_sum = jnp.dot(
        normed, weights_full[:, width : width + units], preferred_element_type=jnp.float32
    )
    hidden = (jax.nn.silu(gate_sum) * up_sum).astype(jnp.bfloat16)
    mlp_part = lax.dot_general(
        hidden,
        weights_full[:, 2 * width : 2 * width + units],
        (((1,), (1,)), ((), ())),
        preferred_element_type=jnp.float32,
    )
    mlp_rows = lax.psum_scatter(
        mlp_part.astype(jnp.bfloat16), "mlp", scatter_dimension=0, tiled=True
    ).astype(jnp.float32)
    return (stream_rows.astype(jnp.float32) + mlp_rows).astype(jnp.bfloat16)


def solution(mesh):
    in_specs = (
        P("req", "mlp"),
        P(("req", "mlp"), None),
        P(("req", "mlp"), None),
        P("req", "mlp", None),
        P("req", "mlp", None),
        P("req"),
        P("req", None),
        P("mlp", None),
        P(),
        P("req", "mlp"),
        P("req", "mlp"),
        P("req", "mlp"),
    )
    out_specs = P(("req", "mlp"), None)
    return jax.shard_map(shards, mesh=mesh, in_specs=in_specs, out_specs=out_specs, check_vma=False)
```

```python
import jax
import jax.numpy as jnp
from jax import lax
from jax.sharding import PartitionSpec as P

H = 32
KVH = 8
HD = 128


norm_eps = 1e-06


def shards(
    queries,
    new_keys,
    new_values,
    cache_keys,
    cache_values,
    cache_len,
    residual,
    out_weight,
    norm_gain,
    gate_weight,
    up_weight,
    down_weight,
):
    n_mlp = lax.axis_size("mlp")
    heads_dev = H // n_mlp
    group_size = H // KVH
    copies = n_mlp // KVH
    assert copies == 2 and heads_dev * copies == group_size
    query_rows = queries.shape[0]
    rows_dev = new_keys.shape[0]
    cache_dev = cache_keys.shape[1]
    cache_half = cache_dev // copies
    new_half = rows_dev // copies
    my_index = lax.axis_index("mlp")
    my_half = my_index % copies

    def to_slots(rows_block, half_rows):
        spread = rows_block.reshape(copies, half_rows, KVH, HD).transpose(1, 2, 0, 3)
        return spread.reshape(half_rows, KVH * copies, HD)

    send = jnp.concatenate(
        [
            to_slots(cache_keys[0], cache_half),
            to_slots(cache_values[0], cache_half),
            to_slots(new_keys, new_half),
            to_slots(new_values, new_half),
        ],
        axis=0,
    )
    arrived = lax.all_to_all(send, "mlp", split_axis=1, concat_axis=0, tiled=True)
    per_src = 2 * cache_half + 2 * new_half
    arrived = arrived.reshape(n_mlp, per_src, HD)
    keys_old = arrived[:, :cache_half].reshape(n_mlp * cache_half, HD)
    values_old = arrived[:, cache_half : 2 * cache_half].reshape(n_mlp * cache_half, HD)
    keys_new = arrived[:, 2 * cache_half : 2 * cache_half + new_half].reshape(n_mlp * new_half, HD)
    values_new = arrived[:, 2 * cache_half + new_half :].reshape(n_mlp * new_half, HD)

    pair = [(d, d ^ 1) for d in range(n_mlp)]
    partner_q = lax.ppermute(queries, "mlp", pair)
    grouped = jnp.concatenate([queries, partner_q], axis=1).reshape(query_rows, group_size, HD)
    score_scale = HD ** (-0.5)

    length = cache_len[0]
    cache_count = n_mlp * cache_half
    keys_all = jnp.concatenate([keys_old, keys_new], axis=0)
    values_all = jnp.concatenate([values_old, values_new], axis=0)
    cached_idx = lax.iota(jnp.int32, cache_count)
    cached_pos = (cached_idx // cache_half) * cache_dev + my_half * cache_half + cached_idx % cache_half
    new_idx = lax.iota(jnp.int32, n_mlp * new_half)
    new_pos = (new_idx // new_half) * rows_dev + my_half * new_half + new_idx % new_half
    token_ids = lax.iota(jnp.int32, query_rows)
    allowed = jnp.concatenate(
        [
            jnp.broadcast_to((cached_pos < length)[None, :], (query_rows, cache_count)),
            new_pos[None, :] <= token_ids[:, None],
        ],
        axis=1,
    )
    scores = (
        jnp.einsum("tqd,kd->qtk", grouped, keys_all, preferred_element_type=jnp.float32)
        * score_scale
    )
    scores = jnp.where(allowed[None], scores, -jnp.inf)
    row_max = jnp.max(scores, axis=-1)
    weights = jnp.exp(scores - row_max[..., None])
    row_sum = jnp.sum(weights, axis=-1)
    weighted = jnp.einsum(
        "qtk,kd->qtd", weights.astype(jnp.bfloat16), values_all, preferred_element_type=jnp.float32
    )

    other_weighted = lax.ppermute(weighted[heads_dev:], "mlp", pair)
    other_stats = lax.ppermute(
        jnp.stack([row_max[heads_dev:], row_sum[heads_dev:]]), "mlp", pair
    )
    other_max = other_stats[0]
    other_sum = other_stats[1]
    mine_max = row_max[:heads_dev]
    top = jnp.maximum(mine_max, other_max)
    scale_a = jnp.exp(mine_max - top)
    scale_b = jnp.exp(other_max - top)
    total = row_sum[:heads_dev] * scale_a + other_sum * scale_b
    mixed = weighted[:heads_dev] * scale_a[..., None] + other_weighted * scale_b[..., None]
    attended = (mixed / total[..., None]).astype(jnp.bfloat16)
    attended = attended.transpose(1, 0, 2).reshape(query_rows, heads_dev * HD)
    partial_value = jnp.dot(attended, out_weight, preferred_element_type=jnp.float32)
    row_start = my_index * rows_dev
    head_sum = lax.psum(partial_value.astype(jnp.bfloat16), "mlp").astype(jnp.float32)
    stream = (residual.astype(jnp.float32) + head_sum).astype(jnp.bfloat16)
    stream_full = stream.astype(jnp.float32)
    factor = lax.rsqrt(jnp.mean(stream_full * stream_full, axis=-1, keepdims=True) + norm_eps)
    normed = (stream_full * factor * norm_gain.astype(jnp.float32)).astype(jnp.bfloat16)
    stream_rows = lax.dynamic_slice_in_dim(stream, row_start, rows_dev, 0)
    units = gate_weight.shape[1]
    width = -(-units // 128) * 128

    def padded(block):
        return jnp.pad(block, ((0, 0), (0, width - units)))

    weights_full = lax.all_gather(
        jnp.concatenate([padded(gate_weight), padded(up_weight), padded(down_weight)], axis=1),
        "req",
        axis=0,
        tiled=True,
    )
    gate_sum = jnp.dot(normed, weights_full[:, :units], preferred_element_type=jnp.float32)
    up_sum = jnp.dot(
        normed, weights_full[:, width : width + units], preferred_element_type=jnp.float32
    )
    hidden = (jax.nn.silu(gate_sum) * up_sum).astype(jnp.bfloat16)
    mlp_part = lax.dot_general(
        hidden,
        weights_full[:, 2 * width : 2 * width + units],
        (((1,), (1,)), ((), ())),
        preferred_element_type=jnp.float32,
    )
    mlp_rows = lax.psum_scatter(
        mlp_part.astype(jnp.bfloat16), "mlp", scatter_dimension=0, tiled=True
    ).astype(jnp.float32)
    return (stream_rows.astype(jnp.float32) + mlp_rows).astype(jnp.bfloat16)


def solution(mesh):
    in_specs = (
        P("req", "mlp"),
        P(("req", "mlp"), None),
        P(("req", "mlp"), None),
        P("req", "mlp", None),
        P("req", "mlp", None),
        P("req"),
        P("req", None),
        P("mlp", None),
        P(),
        P("req", "mlp"),
        P("req", "mlp"),
        P("req", "mlp"),
    )
    out_specs = P(("req", "mlp"), None)
    return jax.shard_map(shards, mesh=mesh, in_specs=in_specs, out_specs=out_specs, check_vma=False)
```

```python
import jax
import jax.numpy as jnp
from jax import lax
from jax.sharding import PartitionSpec as P

H = 32
KVH = 8
HD = 128


norm_eps = 1e-06


def shards(
    queries,
    new_keys,
    new_values,
    cache_keys,
    cache_values,
    cache_len,
    residual,
    out_weight,
    norm_gain,
    gate_weight,
    up_weight,
    down_weight,
):
    n_mlp = lax.axis_size("mlp")
    heads_dev = H // n_mlp
    group_size = H // KVH
    copies = n_mlp // KVH
    assert copies == 2 and heads_dev * copies == group_size
    query_rows = queries.shape[0]
    rows_dev = new_keys.shape[0]
    cache_dev = cache_keys.shape[1]
    cache_half = cache_dev // copies
    new_half = rows_dev // copies
    my_index = lax.axis_index("mlp")
    my_half = my_index % copies

    def to_slots(rows_block, half_rows):
        spread = rows_block.reshape(copies, half_rows, KVH, HD).transpose(1, 2, 0, 3)
        return spread.reshape(half_rows, KVH * copies, HD)

    send = jnp.concatenate(
        [
            to_slots(cache_keys[0], cache_half),
            to_slots(cache_values[0], cache_half),
            to_slots(new_keys, new_half),
            to_slots(new_values, new_half),
        ],
        axis=0,
    )
    arrived = lax.all_to_all(send, "mlp", split_axis=1, concat_axis=0, tiled=True)
    per_src = 2 * cache_half + 2 * new_half
    arrived = arrived.reshape(n_mlp, per_src, HD)
    keys_old = arrived[:, :cache_half].reshape(n_mlp * cache_half, HD)
    values_old = arrived[:, cache_half : 2 * cache_half].reshape(n_mlp * cache_half, HD)
    keys_new = arrived[:, 2 * cache_half : 2 * cache_half + new_half].reshape(n_mlp * new_half, HD)
    values_new = arrived[:, 2 * cache_half + new_half :].reshape(n_mlp * new_half, HD)

    pair = [(d, d ^ 1) for d in range(n_mlp)]
    partner_q = lax.ppermute(queries, "mlp", pair)
    grouped = jnp.concatenate([queries, partner_q], axis=1).reshape(query_rows, group_size, HD)
    score_scale = HD ** (-0.5)

    length = cache_len[0]
    cache_count = n_mlp * cache_half
    keys_all = jnp.concatenate([keys_old, keys_new], axis=0)
    values_all = jnp.concatenate([values_old, values_new], axis=0)
    key_idx = lax.iota(jnp.int32, cache_count + n_mlp * new_half)
    cached_pos = (key_idx // cache_half) * cache_dev + my_half * cache_half + key_idx % cache_half
    new_idx = key_idx - cache_count
    new_pos = (new_idx // new_half) * rows_dev + my_half * new_half + new_idx % new_half
    token_ids = lax.iota(jnp.int32, query_rows)
    allowed = jnp.where(
        (key_idx < cache_count)[None, :],
        (cached_pos < length)[None, :],
        new_pos[None, :] <= token_ids[:, None],
    )
    scores = (
        jnp.einsum("tqd,kd->qtk", grouped, keys_all, preferred_element_type=jnp.float32)
        * score_scale
    )
    scores = jnp.where(allowed[None], scores, -jnp.inf)
    row_max = jnp.max(scores, axis=-1)
    weights = jnp.exp(scores - row_max[..., None])
    row_sum = jnp.sum(weights, axis=-1)
    weighted = jnp.einsum(
        "qtk,kd->qtd", weights.astype(jnp.bfloat16), values_all, preferred_element_type=jnp.float32
    )

    sent = lax.ppermute(
        (weighted[heads_dev:], row_max[heads_dev:], row_sum[heads_dev:]), "mlp", pair
    )
    other_weighted, other_max, other_sum = sent
    mine_max = row_max[:heads_dev]
    top = jnp.maximum(mine_max, other_max)
    scale_a = jnp.exp(mine_max - top)
    scale_b = jnp.exp(other_max - top)
    total = row_sum[:heads_dev] * scale_a + other_sum * scale_b
    mixed = weighted[:heads_dev] * scale_a[..., None] + other_weighted * scale_b[..., None]
    attended = (mixed / total[..., None]).astype(jnp.bfloat16)
    attended = attended.transpose(1, 0, 2).reshape(query_rows, heads_dev * HD)
    partial_value = jnp.dot(attended, out_weight, preferred_element_type=jnp.float32)
    row_start = my_index * rows_dev
    head_sum = lax.psum(partial_value.astype(jnp.bfloat16), "mlp").astype(jnp.float32)
    stream = (residual.astype(jnp.float32) + head_sum).astype(jnp.bfloat16)
    stream_full = stream.astype(jnp.float32)
    factor = lax.rsqrt(jnp.mean(stream_full * stream_full, axis=-1, keepdims=True) + norm_eps)
    normed = (stream_full * factor * norm_gain.astype(jnp.float32)).astype(jnp.bfloat16)
    stream_rows = lax.dynamic_slice_in_dim(stream, row_start, rows_dev, 0)
    units = gate_weight.shape[1]
    width = -(-units // 128) * 128

    def padded(block):
        return jnp.pad(block, ((0, 0), (0, width - units)))

    weights_full = lax.all_gather(
        jnp.concatenate([padded(gate_weight), padded(up_weight), padded(down_weight)], axis=1),
        "req",
        axis=0,
        tiled=True,
    )
    gate_sum = jnp.dot(normed, weights_full[:, :units], preferred_element_type=jnp.float32)
    up_sum = jnp.dot(
        normed, weights_full[:, width : width + units], preferred_element_type=jnp.float32
    )
    hidden = (jax.nn.silu(gate_sum) * up_sum).astype(jnp.bfloat16)
    mlp_part = lax.dot_general(
        hidden,
        weights_full[:, 2 * width : 2 * width + units],
        (((1,), (1,)), ((), ())),
        preferred_element_type=jnp.float32,
    )
    mlp_rows = lax.psum_scatter(
        mlp_part.astype(jnp.bfloat16), "mlp", scatter_dimension=0, tiled=True
    ).astype(jnp.float32)
    return (stream_rows.astype(jnp.float32) + mlp_rows).astype(jnp.bfloat16)


def solution(mesh):
    in_specs = (
        P("req", "mlp"),
        P(("req", "mlp"), None),
        P(("req", "mlp"), None),
        P("req", "mlp", None),
        P("req", "mlp", None),
        P("req"),
        P("req", None),
        P("mlp", None),
        P(),
        P("req", "mlp"),
        P("req", "mlp"),
        P("req", "mlp"),
    )
    out_specs = P(("req", "mlp"), None)
    return jax.shard_map(shards, mesh=mesh, in_specs=in_specs, out_specs=out_specs, check_vma=False)
```

```python
import jax
import jax.numpy as jnp
from jax import lax
from jax.sharding import PartitionSpec as P

H = 32
KVH = 8
HD = 128


norm_eps = 1e-06


def shards(
    queries,
    new_keys,
    new_values,
    cache_keys,
    cache_values,
    cache_len,
    residual,
    out_weight,
    norm_gain,
    gate_weight,
    up_weight,
    down_weight,
):
    n_mlp = lax.axis_size("mlp")
    heads_dev = H // n_mlp
    group_size = H // KVH
    copies = n_mlp // KVH
    assert copies == 2 and heads_dev * copies == group_size
    query_rows = queries.shape[0]
    rows_dev = new_keys.shape[0]
    cache_dev = cache_keys.shape[1]
    cache_half = cache_dev // copies
    new_half = rows_dev // copies
    my_index = lax.axis_index("mlp")
    my_half = my_index % copies

    def to_slots(rows_block, half_rows):
        spread = rows_block.reshape(copies, half_rows, KVH, HD).transpose(1, 2, 0, 3)
        return spread.reshape(half_rows, KVH * copies, HD)

    send = jnp.concatenate(
        [
            to_slots(cache_keys[0], cache_half),
            to_slots(cache_values[0], cache_half),
            to_slots(new_keys, new_half),
            to_slots(new_values, new_half),
        ],
        axis=0,
    )
    arrived = lax.all_to_all(send, "mlp", split_axis=1, concat_axis=0, tiled=True)
    per_src = 2 * cache_half + 2 * new_half
    arrived = arrived.reshape(n_mlp, per_src, HD)
    keys_old = arrived[:, :cache_half].reshape(n_mlp * cache_half, HD)
    values_old = arrived[:, cache_half : 2 * cache_half].reshape(n_mlp * cache_half, HD)
    keys_new = arrived[:, 2 * cache_half : 2 * cache_half + new_half].reshape(n_mlp * new_half, HD)
    values_new = arrived[:, 2 * cache_half + new_half :].reshape(n_mlp * new_half, HD)

    pair = [(d, d ^ 1) for d in range(n_mlp)]
    partner_q = lax.ppermute(queries, "mlp", pair)
    grouped = jnp.concatenate([queries, partner_q], axis=1).reshape(query_rows, group_size, HD)
    score_scale = HD ** (-0.5)

    length = cache_len[0]
    cache_count = n_mlp * cache_half
    keys_all = jnp.concatenate([keys_old, keys_new], axis=0)
    values_all = jnp.concatenate([values_old, values_new], axis=0)
    key_idx = lax.iota(jnp.int32, cache_count + n_mlp * new_half)
    cached_pos = (key_idx // cache_half) * cache_dev + my_half * cache_half + key_idx % cache_half
    new_idx = key_idx - cache_count
    new_pos = (new_idx // new_half) * rows_dev + my_half * new_half + new_idx % new_half
    token_ids = lax.iota(jnp.int32, query_rows)
    allowed = jnp.where(
        (key_idx < cache_count)[None, :],
        (cached_pos < length)[None, :],
        new_pos[None, :] <= token_ids[:, None],
    )
    scores = (
        jnp.einsum("tqd,kd->qtk", grouped, keys_all, preferred_element_type=jnp.float32)
        * score_scale
    )
    scores = jnp.where(allowed[None], scores, -jnp.inf)
    row_max = jnp.max(scores, axis=-1)
    weights = jnp.exp(scores - row_max[..., None])
    row_sum = jnp.sum(weights, axis=-1)
    weighted = jnp.einsum(
        "qtk,kd->qtd", weights.astype(jnp.bfloat16), values_all, preferred_element_type=jnp.float32
    )

    sent = lax.ppermute(
        (weighted[heads_dev:], row_max[heads_dev:], row_sum[heads_dev:]), "mlp", pair
    )
    other_weighted, other_max, other_sum = sent
    mine_max = row_max[:heads_dev]
    top = jnp.maximum(mine_max, other_max)
    scale_a = jnp.exp(mine_max - top)
    scale_b = jnp.exp(other_max - top)
    total = row_sum[:heads_dev] * scale_a + other_sum * scale_b
    mixed = weighted[:heads_dev] * scale_a[..., None] + other_weighted * scale_b[..., None]
    attended = (mixed / total[..., None]).astype(jnp.bfloat16)
    attended = attended.transpose(1, 0, 2).reshape(query_rows, heads_dev * HD)
    partial_value = jnp.dot(attended, out_weight, preferred_element_type=jnp.float32)
    row_start = my_index * rows_dev
    head_sum = lax.psum(partial_value.astype(jnp.bfloat16), "mlp").astype(jnp.float32)
    stream = (residual.astype(jnp.float32) + head_sum).astype(jnp.bfloat16)
    stream_full = stream.astype(jnp.float32)
    factor = lax.rsqrt(jnp.mean(stream_full * stream_full, axis=-1, keepdims=True) + norm_eps)
    normed = (stream_full * factor * norm_gain.astype(jnp.float32)).astype(jnp.bfloat16)
    stream_rows = lax.dynamic_slice_in_dim(stream, row_start, rows_dev, 0)
    units = gate_weight.shape[1]
    width = -(-units // 128) * 128

    def padded(block):
        return jnp.pad(block, ((0, 0), (0, width - units)))

    weights_full = lax.all_gather(
        jnp.concatenate([padded(gate_weight), padded(up_weight), padded(down_weight)], axis=1),
        "req",
        axis=0,
        tiled=True,
    )
    gate_sum = jnp.dot(normed, weights_full[:, :units], preferred_element_type=jnp.float32)
    up_sum = jnp.dot(
        normed, weights_full[:, width : width + units], preferred_element_type=jnp.float32
    )
    hidden = (jax.nn.silu(gate_sum) * up_sum).astype(jnp.bfloat16)
    down_t = lax.optimization_barrier(weights_full[:, 2 * width : 2 * width + units].T)
    mlp_part = jnp.dot(hidden, down_t, preferred_element_type=jnp.float32)
    mlp_rows = lax.psum_scatter(
        mlp_part.astype(jnp.bfloat16), "mlp", scatter_dimension=0, tiled=True
    ).astype(jnp.float32)
    return (stream_rows.astype(jnp.float32) + mlp_rows).astype(jnp.bfloat16)


def solution(mesh):
    in_specs = (
        P("req", "mlp"),
        P(("req", "mlp"), None),
        P(("req", "mlp"), None),
        P("req", "mlp", None),
        P("req", "mlp", None),
        P("req"),
        P("req", None),
        P("mlp", None),
        P(),
        P("req", "mlp"),
        P("req", "mlp"),
        P("req", "mlp"),
    )
    out_specs = P(("req", "mlp"), None)
    return jax.shard_map(shards, mesh=mesh, in_specs=in_specs, out_specs=out_specs, check_vma=False)
```

```python
import jax
import jax.numpy as jnp
from jax import lax
from jax.sharding import PartitionSpec as P

H = 32
KVH = 8
HD = 128


norm_eps = 1e-06


def shards(
    queries,
    new_keys,
    new_values,
    cache_keys,
    cache_values,
    cache_len,
    residual,
    out_weight,
    norm_gain,
    gate_weight,
    up_weight,
    down_weight,
):
    n_mlp = lax.axis_size("mlp")
    heads_dev = H // n_mlp
    group_size = H // KVH
    copies = n_mlp // KVH
    assert copies == 2 and heads_dev * copies == group_size
    query_rows = queries.shape[0]
    rows_dev = new_keys.shape[0]
    cache_dev = cache_keys.shape[1]
    cache_half = cache_dev // copies
    new_half = rows_dev // copies
    my_index = lax.axis_index("mlp")
    my_half = my_index % copies

    def to_slots(rows_block, half_rows):
        spread = rows_block.reshape(copies, half_rows, KVH, HD).transpose(1, 2, 0, 3)
        return spread.reshape(half_rows, KVH * copies, HD)

    send = jnp.concatenate(
        [
            to_slots(cache_keys[0], cache_half),
            to_slots(new_keys, new_half),
            to_slots(cache_values[0], cache_half),
            to_slots(new_values, new_half),
        ],
        axis=0,
    )
    arrived = lax.all_to_all(send, "mlp", split_axis=1, concat_axis=0, tiled=True)
    per_kind = cache_half + new_half
    arrived = arrived.reshape(n_mlp, 2 * per_kind, HD)
    keys_all = arrived[:, :per_kind].reshape(n_mlp * per_kind, HD)
    values_all = arrived[:, per_kind:].reshape(n_mlp * per_kind, HD)

    pair = [(d, d ^ 1) for d in range(n_mlp)]
    partner_q = lax.ppermute(queries, "mlp", pair)
    grouped = jnp.concatenate([queries, partner_q], axis=1).reshape(query_rows, group_size, HD)
    score_scale = HD ** (-0.5)

    length = cache_len[0]
    key_idx = lax.iota(jnp.int32, n_mlp * per_kind)
    source = key_idx // per_kind
    within = key_idx % per_kind
    cached_pos = source * cache_dev + my_half * cache_half + within
    new_pos = source * rows_dev + my_half * new_half + (within - cache_half)
    token_ids = lax.iota(jnp.int32, query_rows)
    allowed = jnp.where(
        (within < cache_half)[None, :],
        (cached_pos < length)[None, :],
        new_pos[None, :] <= token_ids[:, None],
    )
    scores = (
        jnp.einsum("tqd,kd->qtk", grouped, keys_all, preferred_element_type=jnp.float32)
        * score_scale
    )
    scores = jnp.where(allowed[None], scores, -jnp.inf)
    row_max = jnp.max(scores, axis=-1)
    weights = jnp.exp(scores - row_max[..., None])
    row_sum = jnp.sum(weights, axis=-1)
    weighted = jnp.einsum(
        "qtk,kd->qtd", weights.astype(jnp.bfloat16), values_all, preferred_element_type=jnp.float32
    )

    sent = lax.ppermute(
        (weighted[heads_dev:], row_max[heads_dev:], row_sum[heads_dev:]), "mlp", pair
    )
    other_weighted, other_max, other_sum = sent
    mine_max = row_max[:heads_dev]
    top = jnp.maximum(mine_max, other_max)
    scale_a = jnp.exp(mine_max - top)
    scale_b = jnp.exp(other_max - top)
    total = row_sum[:heads_dev] * scale_a + other_sum * scale_b
    mixed = weighted[:heads_dev] * scale_a[..., None] + other_weighted * scale_b[..., None]
    attended = (mixed / total[..., None]).astype(jnp.bfloat16)
    attended = attended.transpose(1, 0, 2).reshape(query_rows, heads_dev * HD)
    partial_value = jnp.dot(attended, out_weight, preferred_element_type=jnp.float32)
    row_start = my_index * rows_dev
    head_sum = lax.psum(partial_value.astype(jnp.bfloat16), "mlp").astype(jnp.float32)
    stream = (residual.astype(jnp.float32) + head_sum).astype(jnp.bfloat16)
    stream_full = stream.astype(jnp.float32)
    factor = lax.rsqrt(jnp.mean(stream_full * stream_full, axis=-1, keepdims=True) + norm_eps)
    normed = (stream_full * factor * norm_gain.astype(jnp.float32)).astype(jnp.bfloat16)
    stream_rows = lax.dynamic_slice_in_dim(stream, row_start, rows_dev, 0)
    units = gate_weight.shape[1]
    width = -(-units // 128) * 128

    def padded(block):
        return jnp.pad(block, ((0, 0), (0, width - units)))

    weights_full = lax.all_gather(
        jnp.concatenate([padded(gate_weight), padded(up_weight), padded(down_weight)], axis=1),
        "req",
        axis=0,
        tiled=True,
    )
    gate_sum = jnp.dot(normed, weights_full[:, :units], preferred_element_type=jnp.float32)
    up_sum = jnp.dot(
        normed, weights_full[:, width : width + units], preferred_element_type=jnp.float32
    )
    hidden = (jax.nn.silu(gate_sum) * up_sum).astype(jnp.bfloat16)
    mlp_part = lax.dot_general(
        hidden,
        weights_full[:, 2 * width : 2 * width + units],
        (((1,), (1,)), ((), ())),
        preferred_element_type=jnp.float32,
    )
    mlp_rows = lax.psum_scatter(
        mlp_part.astype(jnp.bfloat16), "mlp", scatter_dimension=0, tiled=True
    ).astype(jnp.float32)
    return (stream_rows.astype(jnp.float32) + mlp_rows).astype(jnp.bfloat16)


def solution(mesh):
    in_specs = (
        P("req", "mlp"),
        P(("req", "mlp"), None),
        P(("req", "mlp"), None),
        P("req", "mlp", None),
        P("req", "mlp", None),
        P("req"),
        P("req", None),
        P("mlp", None),
        P(),
        P("req", "mlp"),
        P("req", "mlp"),
        P("req", "mlp"),
    )
    out_specs = P(("req", "mlp"), None)
    return jax.shard_map(shards, mesh=mesh, in_specs=in_specs, out_specs=out_specs, check_vma=False)
```

```python
import jax
import jax.numpy as jnp
from jax import lax
from jax.sharding import PartitionSpec as P

H = 32
KVH = 8
HD = 128


norm_eps = 1e-06


def shards(
    queries,
    new_keys,
    new_values,
    cache_keys,
    cache_values,
    cache_len,
    residual,
    out_weight,
    norm_gain,
    gate_weight,
    up_weight,
    down_weight,
):
    n_mlp = lax.axis_size("mlp")
    heads_dev = H // n_mlp
    group_size = H // KVH
    copies = n_mlp // KVH
    assert copies == 2 and heads_dev * copies == group_size
    query_rows = queries.shape[0]
    rows_dev = new_keys.shape[0]
    cache_dev = cache_keys.shape[1]
    cache_half = cache_dev // copies
    new_half = rows_dev // copies
    my_index = lax.axis_index("mlp")
    my_half = my_index % copies

    def to_slots(rows_block, half_rows):
        spread = rows_block.reshape(copies, half_rows, KVH, HD).transpose(1, 2, 0, 3)
        return spread.reshape(half_rows, KVH * copies, HD)

    send = jnp.concatenate(
        [
            to_slots(cache_keys[0], cache_half),
            to_slots(cache_values[0], cache_half),
            to_slots(new_keys, new_half),
            to_slots(new_values, new_half),
        ],
        axis=0,
    )
    arrived = lax.all_to_all(send, "mlp", split_axis=1, concat_axis=0, tiled=True)
    per_src = 2 * cache_half + 2 * new_half
    arrived = arrived.reshape(n_mlp, per_src, HD)
    keys_old = arrived[:, :cache_half].reshape(n_mlp * cache_half, HD)
    values_old = arrived[:, cache_half : 2 * cache_half].reshape(n_mlp * cache_half, HD)
    keys_new = arrived[:, 2 * cache_half : 2 * cache_half + new_half].reshape(n_mlp * new_half, HD)
    values_new = arrived[:, 2 * cache_half + new_half :].reshape(n_mlp * new_half, HD)

    pair = [(d, d ^ 1) for d in range(n_mlp)]
    partner_q = lax.ppermute(queries, "mlp", pair)
    grouped = jnp.concatenate([queries, partner_q], axis=1).reshape(query_rows, group_size, HD)
    score_scale = HD ** (-0.5)

    length = cache_len[0]
    cache_count = n_mlp * cache_half
    keys_all = jnp.concatenate([keys_old, keys_new], axis=0)
    values_all = jnp.concatenate([values_old, values_new], axis=0)
    cached_idx = lax.iota(jnp.int32, cache_count)
    cached_pos = (cached_idx // cache_half) * cache_dev + my_half * cache_half + cached_idx % cache_half
    new_idx = lax.iota(jnp.int32, n_mlp * new_half)
    new_pos = (new_idx // new_half) * rows_dev + my_half * new_half + new_idx % new_half
    token_ids = lax.iota(jnp.int32, query_rows)
    allowed = jnp.concatenate(
        [
            jnp.broadcast_to((cached_pos < length)[None, :], (query_rows, cache_count)),
            new_pos[None, :] <= token_ids[:, None],
        ],
        axis=1,
    )
    scores = (
        jnp.einsum("tqd,kd->qtk", grouped, keys_all, preferred_element_type=jnp.float32)
        * score_scale
    )
    scores = jnp.where(allowed[None], scores, -jnp.inf)
    row_max = jnp.max(scores, axis=-1)
    weights = jnp.exp(scores - row_max[..., None])
    row_sum = jnp.sum(weights, axis=-1)
    weighted = jnp.einsum(
        "qtk,kd->qtd", weights.astype(jnp.bfloat16), values_all, preferred_element_type=jnp.float32
    )

    sent = lax.ppermute(
        (weighted[heads_dev:], row_max[heads_dev:], row_sum[heads_dev:]), "mlp", pair
    )
    other_weighted, other_max, other_sum = sent
    mine_max = row_max[:heads_dev]
    top = jnp.maximum(mine_max, other_max)
    scale_a = jnp.exp(mine_max - top)
    scale_b = jnp.exp(other_max - top)
    total = row_sum[:heads_dev] * scale_a + other_sum * scale_b
    mixed = weighted[:heads_dev] * scale_a[..., None] + other_weighted * scale_b[..., None]
    attended = (mixed / total[..., None]).astype(jnp.bfloat16)
    attended = attended.transpose(1, 0, 2).reshape(query_rows, heads_dev * HD)
    partial_value = jnp.dot(attended, out_weight, preferred_element_type=jnp.float32)
    row_start = my_index * rows_dev
    head_sum = lax.psum(partial_value.astype(jnp.bfloat16), "mlp").astype(jnp.float32)
    stream = (residual.astype(jnp.float32) + head_sum).astype(jnp.bfloat16)
    stream_full = stream.astype(jnp.float32)
    factor = lax.rsqrt(jnp.mean(stream_full * stream_full, axis=-1, keepdims=True) + norm_eps)
    normed = (stream_full * factor * norm_gain.astype(jnp.float32)).astype(jnp.bfloat16)
    stream_rows = lax.dynamic_slice_in_dim(stream, row_start, rows_dev, 0)
    units = gate_weight.shape[1]
    width = -(-units // 128) * 128

    def padded(block):
        return jnp.pad(block, ((0, 0), (0, width - units)))

    weights_full = lax.all_gather(
        jnp.concatenate([padded(gate_weight), padded(up_weight), padded(down_weight)], axis=1),
        "req",
        axis=0,
        tiled=True,
    )
    both = jnp.dot(normed, weights_full[:, : 2 * width], preferred_element_type=jnp.float32)
    gate_sum = both[:, :units]
    up_sum = both[:, width : width + units]
    hidden = (jax.nn.silu(gate_sum) * up_sum).astype(jnp.bfloat16)
    mlp_part = lax.dot_general(
        hidden,
        weights_full[:, 2 * width : 2 * width + units],
        (((1,), (1,)), ((), ())),
        preferred_element_type=jnp.float32,
    )
    mlp_rows = lax.psum_scatter(
        mlp_part.astype(jnp.bfloat16), "mlp", scatter_dimension=0, tiled=True
    ).astype(jnp.float32)
    return (stream_rows.astype(jnp.float32) + mlp_rows).astype(jnp.bfloat16)


def solution(mesh):
    in_specs = (
        P("req", "mlp"),
        P(("req", "mlp"), None),
        P(("req", "mlp"), None),
        P("req", "mlp", None),
        P("req", "mlp", None),
        P("req"),
        P("req", None),
        P("mlp", None),
        P(),
        P("req", "mlp"),
        P("req", "mlp"),
        P("req", "mlp"),
    )
    out_specs = P(("req", "mlp"), None)
    return jax.shard_map(shards, mesh=mesh, in_specs=in_specs, out_specs=out_specs, check_vma=False)
```

```python
import jax
import jax.numpy as jnp
from jax import lax
from jax.sharding import PartitionSpec as P

H = 32
KVH = 8
HD = 128


norm_eps = 1e-06


def shards(
    queries,
    new_keys,
    new_values,
    cache_keys,
    cache_values,
    cache_len,
    residual,
    out_weight,
    norm_gain,
    gate_weight,
    up_weight,
    down_weight,
):
    n_mlp = lax.axis_size("mlp")
    heads_dev = H // n_mlp
    group_size = H // KVH
    copies = n_mlp // KVH
    assert copies == 2 and heads_dev * copies == group_size
    query_rows = queries.shape[0]
    rows_dev = new_keys.shape[0]
    cache_dev = cache_keys.shape[1]
    cache_half = cache_dev // copies
    new_half = rows_dev // copies
    my_index = lax.axis_index("mlp")
    my_half = my_index % copies

    def to_slots(rows_block, half_rows):
        spread = rows_block.reshape(copies, half_rows, KVH, HD).transpose(1, 2, 0, 3)
        return spread.reshape(half_rows, KVH * copies, HD)

    send = jnp.concatenate(
        [
            to_slots(cache_keys[0], cache_half),
            to_slots(cache_values[0], cache_half),
            to_slots(new_keys, new_half),
            to_slots(new_values, new_half),
        ],
        axis=0,
    )
    arrived = lax.all_to_all(send, "mlp", split_axis=1, concat_axis=0, tiled=True)
    per_src = 2 * cache_half + 2 * new_half
    arrived = arrived.reshape(n_mlp, per_src, HD)
    keys_old = arrived[:, :cache_half].reshape(n_mlp * cache_half, HD)
    values_old = arrived[:, cache_half : 2 * cache_half].reshape(n_mlp * cache_half, HD)
    keys_new = arrived[:, 2 * cache_half : 2 * cache_half + new_half].reshape(n_mlp * new_half, HD)
    values_new = arrived[:, 2 * cache_half + new_half :].reshape(n_mlp * new_half, HD)

    pair = [(d, d ^ 1) for d in range(n_mlp)]
    partner_q = lax.ppermute(queries, "mlp", pair)
    grouped = jnp.concatenate([queries, partner_q], axis=1).reshape(query_rows, group_size, HD)
    score_scale = HD ** (-0.5)

    length = cache_len[0]
    cache_count = n_mlp * cache_half
    keys_all = jnp.concatenate([keys_old, keys_new], axis=0)
    values_all = jnp.concatenate([values_old, values_new], axis=0)
    cached_idx = lax.iota(jnp.int32, cache_count)
    cached_pos = (cached_idx // cache_half) * cache_dev + my_half * cache_half + cached_idx % cache_half
    new_idx = lax.iota(jnp.int32, n_mlp * new_half)
    new_pos = (new_idx // new_half) * rows_dev + my_half * new_half + new_idx % new_half
    token_ids = lax.iota(jnp.int32, query_rows)
    allowed = jnp.concatenate(
        [
            jnp.broadcast_to((cached_pos < length)[None, :], (query_rows, cache_count)),
            new_pos[None, :] <= token_ids[:, None],
        ],
        axis=1,
    )
    scores = (
        jnp.einsum("tqd,kd->qtk", grouped, keys_all, preferred_element_type=jnp.float32)
        * score_scale
    )
    scores = jnp.where(allowed[None], scores, -jnp.inf)
    row_max = jnp.max(scores, axis=-1)
    weights = jnp.exp(scores - row_max[..., None])
    row_sum = jnp.sum(weights, axis=-1)
    weighted = jnp.einsum(
        "qtk,kd->qtd", weights.astype(jnp.bfloat16), values_all, preferred_element_type=jnp.float32
    )

    sent = lax.ppermute(
        (weighted[heads_dev:], row_max[heads_dev:], row_sum[heads_dev:]), "mlp", pair
    )
    other_weighted, other_max, other_sum = sent
    mine_max = row_max[:heads_dev]
    top = jnp.maximum(mine_max, other_max)
    scale_a = jnp.exp(mine_max - top)
    scale_b = jnp.exp(other_max - top)
    total = row_sum[:heads_dev] * scale_a + other_sum * scale_b
    mixed = weighted[:heads_dev] * scale_a[..., None] + other_weighted * scale_b[..., None]
    attended = (mixed / total[..., None]).astype(jnp.bfloat16)
    attended = attended.transpose(1, 0, 2).reshape(query_rows, heads_dev * HD)
    partial_value = jnp.dot(attended, out_weight, preferred_element_type=jnp.float32)
    row_start = my_index * rows_dev
    head_sum = lax.psum(partial_value.astype(jnp.bfloat16), "mlp").astype(jnp.float32)
    stream = (residual.astype(jnp.float32) + head_sum).astype(jnp.bfloat16)
    stream_full = stream.astype(jnp.float32)
    factor = lax.rsqrt(jnp.mean(stream_full * stream_full, axis=-1, keepdims=True) + norm_eps)
    normed = (stream_full * factor * norm_gain.astype(jnp.float32)).astype(jnp.bfloat16)
    stream_rows = lax.dynamic_slice_in_dim(stream, row_start, rows_dev, 0)
    units = gate_weight.shape[1]
    width = -(-units // 128) * 128

    def padded(block):
        return jnp.pad(block, ((0, 0), (0, width - units)))

    weights_full = lax.all_gather(
        jnp.concatenate([padded(gate_weight), padded(up_weight), padded(down_weight)], axis=1),
        "req",
        axis=0,
        tiled=True,
    )
    both = jnp.dot(normed, weights_full[:, : 2 * width], preferred_element_type=jnp.float32)
    gate_sum = both[:, :width]
    up_sum = both[:, width:]
    hidden = (jax.nn.silu(gate_sum) * up_sum).astype(jnp.bfloat16)
    mlp_part = lax.dot_general(
        hidden,
        weights_full[:, 2 * width :],
        (((1,), (1,)), ((), ())),
        preferred_element_type=jnp.float32,
    )
    mlp_rows = lax.psum_scatter(
        mlp_part.astype(jnp.bfloat16), "mlp", scatter_dimension=0, tiled=True
    ).astype(jnp.float32)
    return (stream_rows.astype(jnp.float32) + mlp_rows).astype(jnp.bfloat16)


def solution(mesh):
    in_specs = (
        P("req", "mlp"),
        P(("req", "mlp"), None),
        P(("req", "mlp"), None),
        P("req", "mlp", None),
        P("req", "mlp", None),
        P("req"),
        P("req", None),
        P("mlp", None),
        P(),
        P("req", "mlp"),
        P("req", "mlp"),
        P("req", "mlp"),
    )
    out_specs = P(("req", "mlp"), None)
    return jax.shard_map(shards, mesh=mesh, in_specs=in_specs, out_specs=out_specs, check_vma=False)
```
